32 devices in a mesh: beam: 2 (over x), chan: 4 (over y, core), tm: 4 (over z).
Axes of the slice: x: 2, y: 2, z: 4, core: 2. Of those that a mesh axis runs over, the one named last changes fastest.
Arguments:
- samples: float32 [1024, 4096], P(('beam', 'chan'), 'tm'), parts along dimension 0, may hold values from -400 to 400, as said below
- offsets: int32 [9, 512], P(None, 'chan'), may hold values from 0 to 63, as said below
- template_weight: float32 [4, 128], replicated, may hold values from -0.5 to 0.5
- template_taps: int32 [4, 128], replicated, may hold values from 0 to 127, as said below
Outputs:
- matched: float32 [1024, 4, 4096], P(('beam', 'chan'), None, 'tm'), parts along dimension 0
The draws below stay inside these ranges and needn't reach their ends.
There are 2 independent parts, one for each index of `beam`. The reference program is written for one: setup_inputs(seed, part) draws one part's arguments, and reference() takes and returns one part's arrays. A program takes and returns all parts, laid end to end along the dimension named above; an argument that names none is the same for every part. Nothing has to cross between parts.
Inputs may be any that keep to these rules, and one draw needn't show every extreme that they name: samples are finite floats; channel levels and spreads differ. offsets[l, g] is at most min(2^(l + 1), 64) - 1, and reaches that value for some g in every level l. `template_taps`: every template has a tap with lag 128 - 1; lags may repeat.
All inputs are finite; a program needn't handle non-finite values.
Results may differ from the reference program's by a relative error of at most 0.000098.
Values sent between devices are 32-bit elements; how exact they have to be, the bound alone decides.
No kernel may reach another device: no remote copies, remote signals or barrier semaphores. Data moves between devices by JAX's collectives and lax.ppermute only.
A program may use at most 64 MiB of HBM per device.

```python
import math
import jax
import jax.numpy as jnp
from jax import lax

TEMPL = 4
TAPS = 128
SHIFT_CAP = 64
C = 512
TIME = 4096
LEVELS = 9


def draw_samples(key, part):
    subkeys = jax.random.split(key, 4)
    chan_scale = jnp.exp(jax.random.uniform(subkeys[0], (C, 1)) * math.log(10.0))
    baseline = chan_scale * jax.random.uniform(subkeys[1], (C, 1), minval=-2.0, maxval=2.0)
    time_scale = jnp.exp(jax.random.uniform(subkeys[2], (1, TIME)) * math.log(10.0)) / 3.0
    time_ramp = (jnp.arange(TIME, dtype=jnp.float32) / TIME)[None, :]
    envelope = time_scale * jnp.sqrt(0.6 + 1.2 * time_ramp)
    noise_draw = jnp.clip(jax.random.normal(subkeys[3], (C, TIME)), -6.0, 6.0)
    return (baseline * (0.5 + time_ramp) + chan_scale * envelope * noise_draw).astype(jnp.float32)


def draw_offsets(key, part):
    subkeys = jax.random.split(jax.random.fold_in(key, 11), 2)
    level_index = jnp.arange(LEVELS, dtype=jnp.int32)
    window = jnp.minimum(jnp.power(2, level_index + 1), SHIFT_CAP).astype(jnp.int32)
    values = jax.random.randint(subkeys[0], (LEVELS, C), 0, window[:, None])
    marked = jax.random.randint(subkeys[1], (LEVELS, 1), 0, C)
    is_marked = jnp.arange(C, dtype=jnp.int32)[None, :] == marked
    return jnp.where(is_marked, window[:, None] - 1, values).astype(jnp.int32)


def draw_template_taps(key, part):
    subkeys = jax.random.split(jax.random.fold_in(key, 23), 2)
    values = jax.random.randint(subkeys[0], (TEMPL, TAPS), 0, TAPS)
    marked = jax.random.randint(subkeys[1], (TEMPL, 1), 0, TAPS)
    is_marked = jnp.arange(TAPS, dtype=jnp.int32)[None, :] == marked
    return jnp.where(is_marked, TAPS - 1, values).astype(jnp.int32)


def normal_values(stream_key, shape, width, limit, held_as=jnp.bfloat16):
    drawn = jax.random.normal(stream_key, shape, jnp.float32) * width
    return jnp.minimum(jnp.maximum(drawn, -limit), limit).astype(held_as)


def setup_inputs(seed: int = 0, part: int = 0) -> dict:
    splits = jax.random.split(jax.random.key(seed), 5)
    own_keys = jax.random.split(jax.random.fold_in(splits[4], part), 5)
    return {
        "samples": draw_samples(jax.random.fold_in(jax.random.fold_in(splits[4], part), 71), part),
        "offsets": draw_offsets(jax.random.fold_in(splits[4], 71), part),
        "template_weight": normal_values(splits[2], (TEMPL, TAPS), TAPS ** -0.5, 0.5, jnp.float32),
        "template_taps": draw_template_taps(jax.random.fold_in(splits[4], 71), part),
    }


epsilon = 1e-05

def shift_rows(upper_rows, offsets, window):
    length = upper_rows.shape[1]
    padded = jnp.concatenate([upper_rows, jnp.zeros((upper_rows.shape[0], window), jnp.float32)], axis=1)

    def one_row(row_data, offset):
        return lax.dynamic_slice_in_dim(row_data, offset, length)
    return jax.vmap(one_row)(padded, offsets.astype(jnp.int32))

def lag_weights(template_weight, template_taps):
    tap_count = template_weight.shape[1]
    onehot = (template_taps[:, :, None] == jnp.arange(tap_count, dtype=jnp.int32)[None, None, :]).astype(jnp.float32)
    return jnp.einsum('mk,mkl->ml', template_weight, onehot, precision=lax.Precision.HIGHEST)

def make_bands(lag_weight):
    tap_count = lag_weight.shape[1]
    block_len = 2 * tap_count
    inside = jnp.arange(block_len, dtype=jnp.int32)[:, None]
    outside = jnp.arange(block_len, dtype=jnp.int32)[None, :]
    padded = jnp.concatenate([lag_weight, jnp.zeros((lag_weight.shape[0], 1), jnp.float32)], axis=1)

    def lookup_band(offset_gap):
        lookup = jnp.where((offset_gap >= 0) & (offset_gap < tap_count), offset_gap, tap_count)
        return jnp.take(padded, lookup.astype(jnp.int32), axis=1)
    return (lookup_band(inside - outside), lookup_band(inside + block_len - outside))

def filter_blocks(padded_rows, lag_weight):
    band_now, band_next = make_bands(lag_weight)
    row_total, length = padded_rows.shape
    block_len = band_now.shape[1]
    blocks = padded_rows.reshape(row_total, length // block_len, block_len)
    result = jnp.einsum('rni,mit->rmnt', blocks[:, :-1], band_now, precision=lax.Precision.HIGHEST)
    result = result + jnp.einsum('rni,mit->rmnt', blocks[:, 1:], band_next, precision=lax.Precision.HIGHEST)
    return result.reshape(row_total, band_now.shape[0], -1)

def reference(samples, offsets, template_weight, template_taps):
    chan_total, sample_total = samples.shape
    average = lax.optimization_barrier(jnp.sum(samples, axis=1, keepdims=True)) / sample_total
    mean_square = lax.optimization_barrier(jnp.sum(samples * samples, axis=1, keepdims=True)) / sample_total
    scaling = lax.rsqrt(mean_square - average * average + epsilon) / math.sqrt(chan_total)
    spectra = (samples - average) * scaling
    row_count = 1
    for level_index in range(LEVELS):
        window = min(2 ** (level_index + 1), SHIFT_CAP)
        groups = spectra.reshape(chan_total // (2 * row_count), 2, row_count, sample_total)
        lower_rows = jnp.concatenate([groups[:, 0], groups[:, 0]], axis=1).reshape(chan_total, sample_total)
        upper_rows = jnp.concatenate([groups[:, 1], groups[:, 1]], axis=1).reshape(chan_total, sample_total)
        spectra = lower_rows + shift_rows(upper_rows, offsets[level_index], window)
        row_count = row_count * 2
    lag_weight = lag_weights(template_weight, template_taps)
    block_len = 2 * TAPS
    padded = jnp.concatenate([spectra, jnp.zeros((chan_total, block_len), jnp.float32)], axis=1)
    rows_block = min(chan_total, 128)
    row_pieces = padded.reshape(chan_total // rows_block, rows_block, -1)
    result = lax.map(lambda row_piece: filter_blocks(row_piece, lag_weight), row_pieces)
    return result.reshape(chan_total, TEMPL, sample_total)
```

```python
import math

import jax
import jax.numpy as jnp
from jax import lax
from jax.sharding import PartitionSpec as P

SHIFT_CAP = 64


epsilon = 1e-05


def from_behind(value, axis, steps):
    count = lax.axis_size(axis)
    leading, last = (max(0, -steps), min(count, count - steps))
    return lax.ppermute(value, axis, [(source, source + steps) for source in range(leading, last)])


def swapped(block, axis, distance):
    count = lax.axis_size(axis)
    route = []
    for low in range(count):
        high = low | 1 << distance
        if high != low and high < count:
            route += [(low, high), (high, low)]
    return lax.ppermute(block, axis, route)


def butterfly_sum(value, axis):
    count = lax.axis_size(axis)
    if count & (count - 1):
        return lax.psum(value, axis)
    distance = 0
    while 1 << distance < count:
        value = value + swapped(value, axis, distance)
        distance = distance + 1
    return value


def shift_rows(upper_rows, offsets, window):
    current = upper_rows
    stride = 1
    while stride < window:
        chosen = offsets // stride % 2 == 1
        length = current.shape[1] - stride
        current = jnp.where(chosen[:, None], current[:, stride:], current[:, :length])
        stride = stride * 2
    return current


def local_level(spectra, level_offsets, row_count, window):
    row_total, length = spectra.shape
    groups = spectra.reshape(row_total // (2 * row_count), 2, row_count, length)
    lower_half = groups[:, 0]
    upper_half = groups[:, 1]
    lower_half = lower_half[:, :, : length - window + 1]
    lower_rows = jnp.concatenate([lower_half, lower_half], axis=1).reshape(row_total, -1)
    upper_rows = jnp.concatenate([upper_half, upper_half], axis=1).reshape(row_total, -1)
    return lower_rows + shift_rows(upper_rows, level_offsets, window)


def cross_level(spectra, level_offsets, window, bit_index):
    partner = swapped(spectra, "chan", bit_index)
    is_upper = lax.axis_index("chan") // 2**bit_index % 2 == 1
    lower_rows = jnp.where(is_upper, partner, spectra)
    upper_rows = jnp.where(is_upper, spectra, partner)
    lower_rows = lower_rows[:, : spectra.shape[1] - window + 1]
    return lower_rows + shift_rows(upper_rows, level_offsets, window)


def run_tree(spectra, offsets):
    chan_rows = spectra.shape[0]
    local_count = chan_rows.bit_length() - 1
    cross_count = lax.axis_size("chan").bit_length() - 1
    row_count = 1
    for level_index in range(local_count):
        window = min(2 ** (level_index + 1), SHIFT_CAP)
        spectra = local_level(spectra, offsets[level_index], row_count, window)
        row_count = row_count * 2
    for bit_index in range(cross_count):
        level_index = local_count + bit_index
        window = min(2 ** (level_index + 1), SHIFT_CAP)
        spectra = cross_level(spectra, offsets[level_index], window, bit_index)
    return spectra


def lag_weights(template_weight, template_taps):
    tap_count = template_weight.shape[1]
    onehot = (
        template_taps[:, :, None] == jnp.arange(tap_count, dtype=jnp.int32)[None, None, :]
    ).astype(jnp.float32)
    return jnp.einsum("mk,mkl->ml", template_weight, onehot, precision=lax.Precision.HIGHEST)


def toeplitz_band(pattern, block_len):
    templ_count, period = pattern.shape
    tiled = jnp.tile(pattern, (1, block_len))[:, : block_len * (period - 1)]
    rows_view = tiled.reshape(templ_count, block_len, period - 1)[:, :, :block_len]
    return jnp.swapaxes(rows_view, 1, 2)


def make_bands(lag_weight):
    templ_count, tap_count = lag_weight.shape
    block_len = 2 * tap_count
    spare = jnp.zeros((templ_count, block_len - tap_count), jnp.float32)
    empty = jnp.zeros((templ_count, block_len), jnp.float32)
    pattern_now = jnp.concatenate([lag_weight, spare, empty], axis=1)
    pattern_next = jnp.concatenate([empty, lag_weight, spare], axis=1)
    return (toeplitz_band(pattern_now, block_len), toeplitz_band(pattern_next, block_len))


def filter_blocks(padded_rows, lag_weight):
    band_now, band_next = make_bands(lag_weight)
    row_total, length = padded_rows.shape
    block_len = band_now.shape[1]
    blocks = padded_rows.reshape(row_total, length // block_len, block_len)
    result = jnp.einsum("rni,mit->rmnt", blocks[:, :-1], band_now, precision=lax.Precision.HIGHEST)
    result = result + jnp.einsum(
        "rni,mit->rmnt", blocks[:, 1:], band_next, precision=lax.Precision.HIGHEST
    )
    return result.reshape(row_total, band_now.shape[0], -1)


def shards(samples, offsets, template_weight, template_taps):
    chan_rows, time_length = samples.shape
    chan_count = lax.axis_size("chan")
    sample_total = time_length * lax.axis_size("tm")
    totals, squares = butterfly_sum(
        jnp.stack([jnp.sum(samples, axis=1), jnp.sum(samples * samples, axis=1)]), "tm"
    )
    average = totals[:, None] / sample_total
    mean_square = squares[:, None] / sample_total
    scaling = lax.rsqrt(mean_square - average * average + epsilon) / math.sqrt(
        chan_rows * chan_count
    )
    spectra = (samples - average) * scaling
    level_total = (chan_rows * chan_count).bit_length() - 1
    tree_margin = sum(
        (min(2 ** (level_index + 1), SHIFT_CAP) - 1 for level_index in range(level_total))
    )
    filter_margin = template_taps.shape[1] - 1
    edge_samples = from_behind(spectra[:, : tree_margin + filter_margin], "tm", -1)
    spectra = run_tree(jnp.concatenate([spectra, edge_samples], axis=1), offsets)
    lag_weight = lag_weights(template_weight, template_taps)
    block_len = 2 * template_taps.shape[1]
    padded = jnp.concatenate(
        [spectra, jnp.zeros((chan_rows, block_len - filter_margin), jnp.float32)], axis=1
    )
    return filter_blocks(padded, lag_weight)


def solution(mesh):
    in_specs = (P(("beam", "chan"), "tm"), P(None, "chan"), P(), P())
    out_specs = P(("beam", "chan"), None, "tm")
    return jax.shard_map(shards, mesh=mesh, in_specs=in_specs, out_specs=out_specs, check_vma=False)
```

```python
import math

import jax
import jax.numpy as jnp
from jax import lax
from jax.sharding import PartitionSpec as P

SHIFT_CAP = 64


epsilon = 1e-05


def from_behind(value, axis, steps):
    count = lax.axis_size(axis)
    leading, last = (max(0, -steps), min(count, count - steps))
    return lax.ppermute(value, axis, [(source, source + steps) for source in range(leading, last)])


def swapped(block, axis, distance):
    count = lax.axis_size(axis)
    route = []
    for low in range(count):
        high = low | 1 << distance
        if high != low and high < count:
            route += [(low, high), (high, low)]
    return lax.ppermute(block, axis, route)


def butterfly_sum(value, axis):
    count = lax.axis_size(axis)
    if count & (count - 1):
        return lax.psum(value, axis)
    distance = 0
    while 1 << distance < count:
        value = value + swapped(value, axis, distance)
        distance = distance + 1
    return value


def shift_rows(upper_rows, offsets, window):
    current = upper_rows
    stride = 1
    while stride < window:
        chosen = offsets // stride % 2 == 1
        length = current.shape[1] - stride
        current = jnp.where(chosen[:, None], current[:, stride:], current[:, :length])
        stride = stride * 2
    return current


def local_level(spectra, level_offsets, row_count, window):
    row_total, length = spectra.shape
    groups = spectra.reshape(row_total // (2 * row_count), 2, row_count, length)
    lower_half = groups[:, 0]
    upper_half = groups[:, 1]
    lower_half = lower_half[:, :, : length - window + 1]
    lower_rows = jnp.concatenate([lower_half, lower_half], axis=1).reshape(row_total, -1)
    upper_rows = jnp.concatenate([upper_half, upper_half], axis=1).reshape(row_total, -1)
    return lower_rows + shift_rows(upper_rows, level_offsets, window)


def cross_level(spectra, level_offsets, window, bit_index):
    partner = swapped(spectra, "chan", bit_index)
    is_upper = lax.axis_index("chan") // 2**bit_index % 2 == 1
    lower_rows = jnp.where(is_upper, partner, spectra)
    upper_rows = jnp.where(is_upper, spectra, partner)
    lower_rows = lower_rows[:, : spectra.shape[1] - window + 1]
    return lower_rows + shift_rows(upper_rows, level_offsets, window)


def run_tree(spectra, offsets):
    chan_rows = spectra.shape[0]
    local_count = chan_rows.bit_length() - 1
    cross_count = lax.axis_size("chan").bit_length() - 1
    row_count = 1
    for level_index in range(local_count):
        window = min(2 ** (level_index + 1), SHIFT_CAP)
        spectra = local_level(spectra, offsets[level_index], row_count, window)
        row_count = row_count * 2
    for bit_index in range(cross_count):
        level_index = local_count + bit_index
        window = min(2 ** (level_index + 1), SHIFT_CAP)
        spectra = cross_level(spectra, offsets[level_index], window, bit_index)
    return spectra


def lag_weights(template_weight, template_taps):
    tap_count = template_weight.shape[1]
    onehot = (
        template_taps[:, :, None] == jnp.arange(tap_count, dtype=jnp.int32)[None, None, :]
    ).astype(jnp.float32)
    return jnp.einsum("mk,mkl->ml", template_weight, onehot, precision=lax.Precision.HIGHEST)


def make_bands(lag_weight):
    templ_count, tap_count = lag_weight.shape
    block_len = 2 * tap_count
    position = jnp.arange(block_len, dtype=jnp.int32)
    lag = position[:, None] - position[None, :]
    padded = jnp.concatenate([lag_weight, jnp.zeros((templ_count, 1), jnp.float32)], axis=1)

    def band(lag):
        index = jnp.where((lag >= 0) & (lag < tap_count), lag, tap_count)
        return padded[:, index]

    return (band(lag), band(lag + block_len))


def filter_blocks(padded_rows, lag_weight):
    band_now, band_next = make_bands(lag_weight)
    row_total, length = padded_rows.shape
    block_len = band_now.shape[1]
    blocks = padded_rows.reshape(row_total, length // block_len, block_len)
    result = jnp.einsum("rni,mit->rmnt", blocks[:, :-1], band_now, precision=lax.Precision.HIGHEST)
    result = result + jnp.einsum(
        "rni,mit->rmnt", blocks[:, 1:], band_next, precision=lax.Precision.HIGHEST
    )
    return result.reshape(row_total, band_now.shape[0], -1)


def shards(samples, offsets, template_weight, template_taps):
    chan_rows, time_length = samples.shape
    chan_count = lax.axis_size("chan")
    sample_total = time_length * lax.axis_size("tm")
    totals, squares = butterfly_sum(
        jnp.stack([jnp.sum(samples, axis=1), jnp.sum(samples * samples, axis=1)]), "tm"
    )
    average = totals[:, None] / sample_total
    mean_square = squares[:, None] / sample_total
    scaling = lax.rsqrt(mean_square - average * average + epsilon) / math.sqrt(
        chan_rows * chan_count
    )
    spectra = (samples - average) * scaling
    level_total = (chan_rows * chan_count).bit_length() - 1
    tree_margin = sum(
        (min(2 ** (level_index + 1), SHIFT_CAP) - 1 for level_index in range(level_total))
    )
    filter_margin = template_taps.shape[1] - 1
    edge_samples = from_behind(spectra[:, : tree_margin + filter_margin], "tm", -1)
    spectra = run_tree(jnp.concatenate([spectra, edge_samples], axis=1), offsets)
    lag_weight = lag_weights(template_weight, template_taps)
    block_len = 2 * template_taps.shape[1]
    padded = jnp.concatenate(
        [spectra, jnp.zeros((chan_rows, block_len - filter_margin), jnp.float32)], axis=1
    )
    return filter_blocks(padded, lag_weight)


def solution(mesh):
    in_specs = (P(("beam", "chan"), "tm"), P(None, "chan"), P(), P())
    out_specs = P(("beam", "chan"), None, "tm")
    return jax.shard_map(shards, mesh=mesh, in_specs=in_specs, out_specs=out_specs, check_vma=False)
```

```python
import math

import jax
import jax.numpy as jnp
from jax import lax
from jax.sharding import PartitionSpec as P

SHIFT_CAP = 64


epsilon = 1e-05


def from_behind(value, axis, steps):
    count = lax.axis_size(axis)
    leading, last = (max(0, -steps), min(count, count - steps))
    return lax.ppermute(value, axis, [(source, source + steps) for source in range(leading, last)])


def swapped(block, axis, distance):
    count = lax.axis_size(axis)
    route = []
    for low in range(count):
        high = low | 1 << distance
        if high != low and high < count:
            route += [(low, high), (high, low)]
    return lax.ppermute(block, axis, route)


def butterfly_sum(value, axis):
    count = lax.axis_size(axis)
    if count & (count - 1):
        return lax.psum(value, axis)
    distance = 0
    while 1 << distance < count:
        value = value + swapped(value, axis, distance)
        distance = distance + 1
    return value


def shift_rows(upper_rows, offsets, window):
    current = upper_rows
    stride = 1
    while stride < window:
        chosen = offsets // stride % 2 == 1
        length = current.shape[1] - stride
        current = jnp.where(chosen[:, None], current[:, stride:], current[:, :length])
        stride = stride * 2
    return current


def local_level(spectra, level_offsets, row_count, window):
    row_total, length = spectra.shape
    groups = spectra.reshape(row_total // (2 * row_count), 2, row_count, length)
    lower_half = groups[:, 0]
    upper_half = groups[:, 1]
    lower_half = lower_half[:, :, : length - window + 1]
    lower_rows = jnp.concatenate([lower_half, lower_half], axis=1).reshape(row_total, -1)
    upper_rows = jnp.concatenate([upper_half, upper_half], axis=1).reshape(row_total, -1)
    return lower_rows + shift_rows(upper_rows, level_offsets, window)


def cross_level(spectra, level_offsets, window, bit_index):
    partner = swapped(spectra, "chan", bit_index)
    is_upper = lax.axis_index("chan") // 2**bit_index % 2 == 1
    lower_rows = jnp.where(is_upper, partner, spectra)
    upper_rows = jnp.where(is_upper, spectra, partner)
    lower_rows = lower_rows[:, : spectra.shape[1] - window + 1]
    return lower_rows + shift_rows(upper_rows, level_offsets, window)


def run_tree(spectra, offsets):
    chan_rows = spectra.shape[0]
    local_count = chan_rows.bit_length() - 1
    cross_count = lax.axis_size("chan").bit_length() - 1
    row_count = 1
    for level_index in range(local_count):
        window = min(2 ** (level_index + 1), SHIFT_CAP)
        spectra = local_level(spectra, offsets[level_index], row_count, window)
        row_count = row_count * 2
    for bit_index in range(cross_count):
        level_index = local_count + bit_index
        window = min(2 ** (level_index + 1), SHIFT_CAP)
        spectra = cross_level(spectra, offsets[level_index], window, bit_index)
    return spectra


def lag_weights(template_weight, template_taps):
    tap_count = template_weight.shape[1]
    onehot = (
        template_taps[:, :, None] == jnp.arange(tap_count, dtype=jnp.int32)[None, None, :]
    ).astype(jnp.float32)
    return jnp.einsum("mk,mkl->ml", template_weight, onehot, precision=lax.Precision.HIGHEST)


def skewed(pattern, block_len):
    templ_count, length = pattern.shape
    current = jnp.broadcast_to(pattern[:, None, :], (templ_count, block_len, length))
    offsets = block_len - 1 - jnp.arange(block_len, dtype=jnp.int32)
    stride = 1
    while stride < block_len:
        chosen = (offsets // stride % 2 == 1)[None, :, None]
        length = current.shape[2] - stride
        current = jnp.where(chosen, current[:, :, stride:], current[:, :, :length])
        stride = stride * 2
    return current


def make_bands(lag_weight):
    templ_count, tap_count = lag_weight.shape
    block_len = 2 * tap_count
    span = 2 * block_len - 1
    lead = jnp.zeros((templ_count, block_len - 1), jnp.float32)
    pattern_now = jnp.concatenate(
        [lead, lag_weight, jnp.zeros((templ_count, span - block_len + 1 - tap_count), jnp.float32)],
        axis=1,
    )
    pattern_next = jnp.concatenate(
        [lag_weight[:, 1:], jnp.zeros((templ_count, span - tap_count + 1), jnp.float32)], axis=1
    )
    return (skewed(pattern_now, block_len), skewed(pattern_next, block_len))


def filter_blocks(padded_rows, lag_weight):
    band_now, band_next = make_bands(lag_weight)
    row_total, length = padded_rows.shape
    block_len = band_now.shape[1]
    blocks = padded_rows.reshape(row_total, length // block_len, block_len)
    result = jnp.einsum("rni,mti->rmnt", blocks[:, :-1], band_now, precision=lax.Precision.HIGHEST)
    result = result + jnp.einsum(
        "rni,mti->rmnt", blocks[:, 1:], band_next, precision=lax.Precision.HIGHEST
    )
    return result.reshape(row_total, band_now.shape[0], -1)


def shards(samples, offsets, template_weight, template_taps):
    chan_rows, time_length = samples.shape
    chan_count = lax.axis_size("chan")
    sample_total = time_length * lax.axis_size("tm")
    totals, squares = butterfly_sum(
        jnp.stack([jnp.sum(samples, axis=1), jnp.sum(samples * samples, axis=1)]), "tm"
    )
    average = totals[:, None] / sample_total
    mean_square = squares[:, None] / sample_total
    scaling = lax.rsqrt(mean_square - average * average + epsilon) / math.sqrt(
        chan_rows * chan_count
    )
    spectra = (samples - average) * scaling
    level_total = (chan_rows * chan_count).bit_length() - 1
    tree_margin = sum(
        (min(2 ** (level_index + 1), SHIFT_CAP) - 1 for level_index in range(level_total))
    )
    filter_margin = template_taps.shape[1] - 1
    edge_samples = from_behind(spectra[:, : tree_margin + filter_margin], "tm", -1)
    spectra = run_tree(jnp.concatenate([spectra, edge_samples], axis=1), offsets)
    lag_weight = lag_weights(template_weight, template_taps)
    block_len = 2 * template_taps.shape[1]
    padded = jnp.concatenate(
        [spectra, jnp.zeros((chan_rows, block_len - filter_margin), jnp.float32)], axis=1
    )
    return filter_blocks(padded, lag_weight)


def solution(mesh):
    in_specs = (P(("beam", "chan"), "tm"), P(None, "chan"), P(), P())
    out_specs = P(("beam", "chan"), None, "tm")
    return jax.shard_map(shards, mesh=mesh, in_specs=in_specs, out_specs=out_specs, check_vma=False)
```

```python
import math

import jax
import jax.numpy as jnp
from jax import lax
from jax.sharding import PartitionSpec as P

SHIFT_CAP = 64


epsilon = 1e-05


def from_behind(value, axis, steps):
    count = lax.axis_size(axis)
    leading, last = (max(0, -steps), min(count, count - steps))
    return lax.ppermute(value, axis, [(source, source + steps) for source in range(leading, last)])


def swapped(block, axis, distance):
    count = lax.axis_size(axis)
    route = []
    for low in range(count):
        high = low | 1 << distance
        if high != low and high < count:
            route += [(low, high), (high, low)]
    return lax.ppermute(block, axis, route)


def butterfly_sum(value, axis):
    count = lax.axis_size(axis)
    if count & (count - 1):
        return lax.psum(value, axis)
    distance = 0
    while 1 << distance < count:
        value = value + swapped(value, axis, distance)
        distance = distance + 1
    return value


def shift_rows(upper_rows, offsets, window):
    current = upper_rows
    stride = 1
    while stride < window:
        chosen = offsets // stride % 2 == 1
        length = current.shape[1] - stride
        current = jnp.where(chosen[:, None], current[:, stride:], current[:, :length])
        stride = stride * 2
    return current


def local_level(spectra, level_offsets, row_count, window):
    row_total, length = spectra.shape
    groups = spectra.reshape(row_total // (2 * row_count), 2, row_count, length)
    lower_half = groups[:, 0]
    upper_half = groups[:, 1]
    lower_half = lower_half[:, :, : length - window + 1]
    lower_rows = jnp.concatenate([lower_half, lower_half], axis=1).reshape(row_total, -1)
    upper_rows = jnp.concatenate([upper_half, upper_half], axis=1).reshape(row_total, -1)
    return lower_rows + shift_rows(upper_rows, level_offsets, window)


def cross_level(spectra, level_offsets, window, bit_index):
    partner = swapped(spectra, "chan", bit_index)
    is_upper = lax.axis_index("chan") // 2**bit_index % 2 == 1
    lower_rows = jnp.where(is_upper, partner, spectra)
    upper_rows = jnp.where(is_upper, spectra, partner)
    lower_rows = lower_rows[:, : spectra.shape[1] - window + 1]
    return lower_rows + shift_rows(upper_rows, level_offsets, window)


def run_tree(spectra, offsets):
    chan_rows = spectra.shape[0]
    local_count = chan_rows.bit_length() - 1
    cross_count = lax.axis_size("chan").bit_length() - 1
    row_count = 1
    for level_index in range(local_count):
        window = min(2 ** (level_index + 1), SHIFT_CAP)
        spectra = local_level(spectra, offsets[level_index], row_count, window)
        row_count = row_count * 2
    for bit_index in range(cross_count):
        level_index = local_count + bit_index
        window = min(2 ** (level_index + 1), SHIFT_CAP)
        spectra = cross_level(spectra, offsets[level_index], window, bit_index)
    return spectra


def lag_weights(template_weight, template_taps):
    tap_count = template_weight.shape[1]
    onehot = (
        template_taps[:, :, None] == jnp.arange(tap_count, dtype=jnp.int32)[None, None, :]
    ).astype(jnp.float32)
    return jnp.einsum("mk,mkl->ml", template_weight, onehot, precision=lax.Precision.HIGHEST)


def toeplitz_band(pattern, block_len):
    templ_count, period = pattern.shape
    tiled = jnp.tile(pattern, (1, block_len))[:, : block_len * (period - 1)]
    rows_view = tiled.reshape(templ_count, block_len, period - 1)[:, :, :block_len]
    return jnp.swapaxes(rows_view, 1, 2)


def make_bands(lag_weight):
    templ_count, tap_count = lag_weight.shape
    block_len = 2 * tap_count
    spare = jnp.zeros((templ_count, block_len - tap_count), jnp.float32)
    empty = jnp.zeros((templ_count, block_len), jnp.float32)
    pattern_now = jnp.concatenate([lag_weight, spare, empty], axis=1)
    pattern_next = jnp.concatenate([empty, lag_weight, spare], axis=1)
    return (toeplitz_band(pattern_now, block_len), toeplitz_band(pattern_next, block_len))


def filter_blocks(padded_rows, lag_weight):
    band_now, band_next = make_bands(lag_weight)
    row_total, length = padded_rows.shape
    block_len = band_now.shape[1]
    blocks = padded_rows.reshape(row_total, length // block_len, block_len)
    windows = jnp.concatenate([blocks[:, :-1], blocks[:, 1:]], axis=2)
    band = jnp.concatenate([band_now, band_next], axis=1)
    result = jnp.einsum("rni,mit->rmnt", windows, band, precision=lax.Precision.HIGHEST)
    return result.reshape(row_total, band_now.shape[0], -1)


def shards(samples, offsets, template_weight, template_taps):
    chan_rows, time_length = samples.shape
    chan_count = lax.axis_size("chan")
    sample_total = time_length * lax.axis_size("tm")
    totals, squares = butterfly_sum(
        jnp.stack([jnp.sum(samples, axis=1), jnp.sum(samples * samples, axis=1)]), "tm"
    )
    average = totals[:, None] / sample_total
    mean_square = squares[:, None] / sample_total
    scaling = lax.rsqrt(mean_square - average * average + epsilon) / math.sqrt(
        chan_rows * chan_count
    )
    spectra = (samples - average) * scaling
    level_total = (chan_rows * chan_count).bit_length() - 1
    tree_margin = sum(
        (min(2 ** (level_index + 1), SHIFT_CAP) - 1 for level_index in range(level_total))
    )
    filter_margin = template_taps.shape[1] - 1
    edge_samples = from_behind(spectra[:, : tree_margin + filter_margin], "tm", -1)
    spectra = run_tree(jnp.concatenate([spectra, edge_samples], axis=1), offsets)
    lag_weight = lag_weights(template_weight, template_taps)
    block_len = 2 * template_taps.shape[1]
    padded = jnp.concatenate(
        [spectra, jnp.zeros((chan_rows, block_len - filter_margin), jnp.float32)], axis=1
    )
    return filter_blocks(padded, lag_weight)


def solution(mesh):
    in_specs = (P(("beam", "chan"), "tm"), P(None, "chan"), P(), P())
    out_specs = P(("beam", "chan"), None, "tm")
    return jax.shard_map(shards, mesh=mesh, in_specs=in_specs, out_specs=out_specs, check_vma=False)
```

```python
import math

import jax
import jax.numpy as jnp
from jax import lax
from jax.sharding import PartitionSpec as P

SHIFT_CAP = 64


epsilon = 1e-05


def from_behind(value, axis, steps):
    count = lax.axis_size(axis)
    leading, last = (max(0, -steps), min(count, count - steps))
    return lax.ppermute(value, axis, [(source, source + steps) for source in range(leading, last)])


def swapped(block, axis, distance):
    count = lax.axis_size(axis)
    route = []
    for low in range(count):
        high = low | 1 << distance
        if high != low and high < count:
            route += [(low, high), (high, low)]
    return lax.ppermute(block, axis, route)


def butterfly_sum(value, axis):
    count = lax.axis_size(axis)
    total = value
    for step in range(1, count):
        route = [(source, (source + step) % count) for source in range(count)]
        total = total + lax.ppermute(value, axis, route)
    return total


def shift_rows(upper_rows, offsets, window):
    current = upper_rows
    stride = 1
    while stride < window:
        chosen = offsets // stride % 2 == 1
        length = current.shape[1] - stride
        current = jnp.where(chosen[:, None], current[:, stride:], current[:, :length])
        stride = stride * 2
    return current


def local_level(spectra, level_offsets, row_count, window):
    row_total, length = spectra.shape
    groups = spectra.reshape(row_total // (2 * row_count), 2, row_count, length)
    lower_half = groups[:, 0]
    upper_half = groups[:, 1]
    lower_half = lower_half[:, :, : length - window + 1]
    lower_rows = jnp.concatenate([lower_half, lower_half], axis=1).reshape(row_total, -1)
    upper_rows = jnp.concatenate([upper_half, upper_half], axis=1).reshape(row_total, -1)
    return lower_rows + shift_rows(upper_rows, level_offsets, window)


def cross_level(spectra, level_offsets, window, bit_index):
    partner = swapped(spectra, "chan", bit_index)
    is_upper = lax.axis_index("chan") // 2**bit_index % 2 == 1
    lower_rows = jnp.where(is_upper, partner, spectra)
    upper_rows = jnp.where(is_upper, spectra, partner)
    lower_rows = lower_rows[:, : spectra.shape[1] - window + 1]
    return lower_rows + shift_rows(upper_rows, level_offsets, window)


def run_tree(spectra, offsets):
    chan_rows = spectra.shape[0]
    local_count = chan_rows.bit_length() - 1
    cross_count = lax.axis_size("chan").bit_length() - 1
    row_count = 1
    for level_index in range(local_count):
        window = min(2 ** (level_index + 1), SHIFT_CAP)
        spectra = local_level(spectra, offsets[level_index], row_count, window)
        row_count = row_count * 2
    for bit_index in range(cross_count):
        level_index = local_count + bit_index
        window = min(2 ** (level_index + 1), SHIFT_CAP)
        spectra = cross_level(spectra, offsets[level_index], window, bit_index)
    return spectra


def lag_weights(template_weight, template_taps):
    tap_count = template_weight.shape[1]
    onehot = (
        template_taps[:, :, None] == jnp.arange(tap_count, dtype=jnp.int32)[None, None, :]
    ).astype(jnp.float32)
    return jnp.einsum("mk,mkl->ml", template_weight, onehot, precision=lax.Precision.HIGHEST)


def toeplitz_band(pattern, block_len):
    templ_count, period = pattern.shape
    tiled = jnp.tile(pattern, (1, block_len))[:, : block_len * (period - 1)]
    rows_view = tiled.reshape(templ_count, block_len, period - 1)[:, :, :block_len]
    return jnp.swapaxes(rows_view, 1, 2)


def make_bands(lag_weight):
    templ_count, tap_count = lag_weight.shape
    block_len = 2 * tap_count
    spare = jnp.zeros((templ_count, block_len - tap_count), jnp.float32)
    empty = jnp.zeros((templ_count, block_len), jnp.float32)
    pattern_now = jnp.concatenate([lag_weight, spare, empty], axis=1)
    pattern_next = jnp.concatenate([empty, lag_weight, spare], axis=1)
    return (toeplitz_band(pattern_now, block_len), toeplitz_band(pattern_next, block_len))


def filter_blocks(padded_rows, lag_weight):
    band_now, band_next = make_bands(lag_weight)
    row_total, length = padded_rows.shape
    block_len = band_now.shape[1]
    blocks = padded_rows.reshape(row_total, length // block_len, block_len)
    result = jnp.einsum("rni,mit->rmnt", blocks[:, :-1], band_now, precision=lax.Precision.HIGHEST)
    result = result + jnp.einsum(
        "rni,mit->rmnt", blocks[:, 1:], band_next, precision=lax.Precision.HIGHEST
    )
    return result.reshape(row_total, band_now.shape[0], -1)


def shards(samples, offsets, template_weight, template_taps):
    chan_rows, time_length = samples.shape
    chan_count = lax.axis_size("chan")
    sample_total = time_length * lax.axis_size("tm")
    totals, squares = butterfly_sum(
        jnp.stack([jnp.sum(samples, axis=1), jnp.sum(samples * samples, axis=1)]), "tm"
    )
    average = totals[:, None] / sample_total
    mean_square = squares[:, None] / sample_total
    scaling = lax.rsqrt(mean_square - average * average + epsilon) / math.sqrt(
        chan_rows * chan_count
    )
    spectra = (samples - average) * scaling
    level_total = (chan_rows * chan_count).bit_length() - 1
    tree_margin = sum(
        (min(2 ** (level_index + 1), SHIFT_CAP) - 1 for level_index in range(level_total))
    )
    filter_margin = template_taps.shape[1] - 1
    edge_samples = from_behind(spectra[:, : tree_margin + filter_margin], "tm", -1)
    spectra = run_tree(jnp.concatenate([spectra, edge_samples], axis=1), offsets)
    lag_weight = lag_weights(template_weight, template_taps)
    block_len = 2 * template_taps.shape[1]
    padded = jnp.concatenate(
        [spectra, jnp.zeros((chan_rows, block_len - filter_margin), jnp.float32)], axis=1
    )
    return filter_blocks(padded, lag_weight)


def solution(mesh):
    in_specs = (P(("beam", "chan"), "tm"), P(None, "chan"), P(), P())
    out_specs = P(("beam", "chan"), None, "tm")
    return jax.shard_map(shards, mesh=mesh, in_specs=in_specs, out_specs=out_specs, check_vma=False)
```
